256 devices in a mesh: dom: 32 (over y, x, core), mem: 8 (over z).
Axes of the slice: x: 4, y: 4, z: 8, core: 2. Of those that a mesh axis runs over, the one named last changes fastest.
Arguments:
- global_latent: bfloat16 [65536, 512], P('dom'), may hold values from -6 to 6
- send_rows: int32 [32, 3, 256], P('dom'), may hold values from 0 to 2047
- regional: bfloat16 [8, 8192, 512], P('mem', 'dom'), may hold values from -6 to 6
- interp_index: int32 [8192, 4], P('dom'), may hold values from 0 to 767
- interp_weight: float32 [8192, 4], P('dom'), may hold values from 0 to 1
- neighbors: int32 [64, 4], P('dom'), may hold values from 0 to 3
- w_bound: bfloat16 [512, 512], replicated, may hold values from -0.25 to 0.25
- w_query: bfloat16 [512, 512], replicated, may hold values from -0.25 to 0.25
- w_key: bfloat16 [512, 512], replicated, may hold values from -0.25 to 0.25
- w_value: bfloat16 [512, 512], replicated, may hold values from -0.25 to 0.25
- w_output: bfloat16 [512, 512], replicated, may hold values from -0.25 to 0.25
- norm_gain: float32 [512], replicated, may hold values from 0.5 to 2
- cotangent: bfloat16 [8, 8192, 512], P('mem', 'dom'), may hold values from -0.0625 to 0.0625
Outputs:
- regional_out: bfloat16 [8, 8192, 512], P('mem', 'dom')
- grad_query: float32 [512, 512], replicated
- grad_key: float32 [512, 512], replicated
- grad_value: float32 [512, 512], replicated
- grad_output: float32 [512, 512], replicated
- grad_bound: float32 [512, 512], replicated
- grad_gain: float32 [512], replicated
The draws below stay inside these ranges and needn't reach their ends.
Inputs may be any that keep to these rules, and one draw needn't show every extreme that they name: `send_rows`: row numbers within the sending band. `interp_index`: slots of the cell's own tile's forcing table. `neighbors`: extended block numbers: 0 is the block before the tile, 3 the block after it.
All inputs are finite; a program needn't handle non-finite values.
Results may differ from the reference program's by a relative error of at most 0.015.
Values may be sent and summed in bfloat16 or wider, within the bound.
No kernel may reach another device: no remote copies, remote signals or barrier semaphores. Data moves between devices by JAX's collectives and lax.ppermute only.
A program may use at most 64 MiB of HBM per device.

```python
import math
import jax
import jax.numpy as jnp
from jax import lax

W = 512
HEADS = 8
BLK = 128
NBR = 4
KPT = 4
GROW_DEV = 2048
REG_DEV = 256
CAP = 256
MEMBERS = 8
GROWS = 65536
RCELLS = 8192
NB_DEV = 2
NBLOCKS = 64
SLOTS = 768
N_DOM = 32


def touch_ends(drawn, own_key, smallest, largest):
    longest = drawn.shape.index(max(drawn.shape))
    spots = []
    for shift in (0, 1):
        where = [jax.random.randint(jax.random.fold_in(own_key, axis), (), 0, length) for axis, length in enumerate(drawn.shape)]
        where[longest] = (where[longest] + shift) % drawn.shape[longest]
        spots.append(tuple(where))
    return drawn.at[spots[0]].set(smallest).at[spots[1]].set(largest)


def levels(key, shape, pieces, low, top_value):
    gain = 1.0
    for position, blocks in pieces:
        steps = jax.random.uniform(jax.random.fold_in(jax.random.fold_in(key, 6), position), (blocks,), jnp.float32, low / len(pieces), top_value / len(pieces))
        gain = gain * jnp.repeat(jnp.exp(steps), shape[position] // blocks).reshape((-1,) + (1,) * (len(shape) - 1 - position))
    return gain


def centred(stream_key, extent, deviation, limit, pieces=(), dtype=jnp.bfloat16):
    factor_of = levels(stream_key, extent, pieces, -0.22, 0.18) if pieces else 1.0
    values = jax.random.normal(stream_key, extent, jnp.float32) * deviation * factor_of
    return jnp.minimum(jnp.maximum(values, -limit), limit).astype(dtype)


def setup_inputs(seed: int = 0) -> dict:
    key_list = jax.random.split(jax.random.key(seed), 14)
    return {
        "global_latent": centred(key_list[0], (GROWS, W), 1.0, 6.0, ((0, 32),)),
        "send_rows": touch_ends(jax.random.randint(key_list[1], (N_DOM, 3, CAP), 0, GROW_DEV), jax.random.fold_in(key_list[1], 1), 0, GROW_DEV - 1).astype(jnp.int32),
        "regional": centred(key_list[2], (MEMBERS, RCELLS, W), 1.0, 6.0, ((0, 8), (1, 32))),
        "interp_index": touch_ends(jax.random.randint(key_list[3], (RCELLS, KPT), 0, SLOTS), jax.random.fold_in(key_list[3], 1), 0, SLOTS - 1).astype(jnp.int32),
        "interp_weight": jnp.clip(1.0 * jax.random.uniform(key_list[4], (RCELLS, KPT), jnp.float32) ** levels(key_list[4], (RCELLS, KPT), ((0, 32),), -0.2, 0.2), 0.0, 1.0),
        "neighbors": touch_ends(jax.random.randint(key_list[5], (NBLOCKS, NBR), 0, NB_DEV + 2), jax.random.fold_in(key_list[5], 1), 0, (NB_DEV + 2) - 1).astype(jnp.int32),
        "w_bound": centred(key_list[6], (W, W), W ** -0.5, 0.25),
        "w_query": centred(key_list[7], (W, W), W ** -0.5, 0.25),
        "w_key": centred(key_list[8], (W, W), W ** -0.5, 0.25),
        "w_value": centred(key_list[9], (W, W), W ** -0.5, 0.25),
        "w_output": centred(key_list[10], (W, W), W ** -0.5, 0.25),
        "norm_gain": jnp.clip(jnp.exp(jax.random.uniform(key_list[11], (W,), jnp.float32, math.log(0.5), math.log(2.0))), 0.5, 2.0),
        "cotangent": centred(key_list[12], (MEMBERS, RCELLS, W), (1.0 / (MEMBERS * RCELLS) ** 0.5), 0.0625, ((0, 8), (1, 32))),
    }


def normalize(forced, norm_gain):
    inverse = lax.rsqrt(lax.optimization_barrier(jnp.mean(forced * forced, axis=-1, keepdims=True)) + 1e-06)
    return (forced * inverse * norm_gain).astype(jnp.bfloat16)

def attend_core(queries, key_rows, value_rows, neighbors):
    blocks = queries.shape[0] // BLK
    head_dim = W // HEADS
    query_blocks = queries.reshape(blocks, BLK, HEADS, head_dim).astype(jnp.float32)
    key_blocks = key_rows.reshape(blocks + 2, BLK, W)[neighbors].reshape(blocks, NBR * BLK, HEADS, head_dim).astype(jnp.float32)
    value_blocks = value_rows.reshape(blocks + 2, BLK, W)[neighbors].reshape(blocks, NBR * BLK, HEADS, head_dim).astype(jnp.float32)
    scores = jnp.einsum('bqhd,bkhd->bhqk', query_blocks, key_blocks) * (1.0 / math.sqrt(head_dim))
    expo = jnp.exp(scores)
    probs = (expo / lax.optimization_barrier(jnp.sum(expo, axis=-1, keepdims=True))).astype(jnp.bfloat16)
    mixed = jnp.einsum('bhqk,bkhd->bqhd', probs.astype(jnp.float32), value_blocks)
    return mixed.reshape(blocks * BLK, W).astype(jnp.bfloat16)

def tile_pass(hidden, extended, neighbors, grads_out, w_query, w_key, w_value, w_output):
    queries = jnp.dot(hidden, w_query, preferred_element_type=jnp.float32).astype(jnp.bfloat16)
    key_rows = jnp.dot(extended, w_key, preferred_element_type=jnp.float32).astype(jnp.bfloat16)
    value_rows = jnp.dot(extended, w_value, preferred_element_type=jnp.float32).astype(jnp.bfloat16)

    def core(first, second, third):
        return attend_core(first, second, third, neighbors)
    mixed_heads, core_back = jax.vjp(core, queries, key_rows, value_rows)
    attended = jnp.dot(mixed_heads, w_output, preferred_element_type=jnp.float32)
    grad_output = jnp.dot(mixed_heads.T, grads_out, preferred_element_type=jnp.float32)
    g_mixed = jnp.dot(grads_out, w_output.T, preferred_element_type=jnp.float32).astype(jnp.bfloat16)
    g_queries, g_keys, g_values = core_back(g_mixed)
    grad_query = jnp.dot(hidden.T, g_queries, preferred_element_type=jnp.float32)
    grad_key = jnp.dot(extended.T, g_keys, preferred_element_type=jnp.float32)
    grad_value = jnp.dot(extended.T, g_values, preferred_element_type=jnp.float32)
    g_hidden = jnp.dot(g_queries, w_query.T, preferred_element_type=jnp.float32)
    g_extended = jnp.dot(g_keys, w_key.T, preferred_element_type=jnp.float32) + jnp.dot(g_values, w_value.T, preferred_element_type=jnp.float32)
    return (attended, g_hidden, g_extended, grad_query, grad_key, grad_value, grad_output)

def make_boundary(global_latent, send_rows, interp_index, interp_weight):
    bands = global_latent.reshape(N_DOM, GROW_DEV, W)

    def pick(band_rows, row_list):
        return band_rows[row_list]
    picked = jax.vmap(pick)(bands, send_rows)
    from_below = jnp.roll(picked[:, 2], 1, axis=0)
    from_above = jnp.roll(picked[:, 0], -1, axis=0)
    tables = jnp.concatenate([from_below, picked[:, 1], from_above], axis=1)
    index_tiles = interp_index.reshape(N_DOM, REG_DEV, KPT)
    weight_tiles = interp_weight.reshape(N_DOM, REG_DEV, KPT)

    def one_tile(packed):
        table, index_rows, weight_rows = packed
        return lax.optimization_barrier(jnp.sum(weight_rows[:, :, None] * table[index_rows].astype(jnp.float32), axis=1)).astype(jnp.bfloat16)
    return lax.map(one_tile, (tables, index_tiles, weight_tiles)).reshape(RCELLS, W)

def reference(global_latent, send_rows, regional, interp_index, interp_weight, neighbors, w_bound, w_query, w_key, w_value, w_output, norm_gain, cotangent):
    boundary = make_boundary(global_latent, send_rows, interp_index, interp_weight)
    projected = jnp.dot(boundary, w_bound, preferred_element_type=jnp.float32)
    neighbor_tiles = neighbors.reshape(N_DOM, NB_DEV, NBR)

    def member(totals, packed):
        regional_m, cot_m = packed
        forced = regional_m.astype(jnp.float32) + projected
        hidden, norm_back = jax.vjp(normalize, forced, norm_gain)
        tile_rows = hidden.reshape(N_DOM, REG_DEV, W)
        zero_block = jnp.zeros((1, BLK, W), jnp.bfloat16)
        below_rim = jnp.concatenate([zero_block, tile_rows[:-1, REG_DEV - BLK:]], axis=0)
        above_rim = jnp.concatenate([tile_rows[1:, :BLK], zero_block], axis=0)
        extended = jnp.concatenate([below_rim, tile_rows, above_rim], axis=1)
        cot_tiles = cot_m.reshape(N_DOM, REG_DEV, W)

        def run_tile(items):
            return tile_pass(items[0], items[1], items[2], items[3], w_query, w_key, w_value, w_output)
        attended, g_hidden, g_extended, gq, gk, gv, go = lax.map(run_tile, (tile_rows, extended, neighbor_tiles, cot_tiles))
        g_tiles = g_hidden + g_extended[:, BLK:BLK + REG_DEV]
        zero_grad = jnp.zeros((1, BLK, W), jnp.float32)
        from_before = jnp.concatenate([zero_grad, g_extended[:-1, BLK + REG_DEV:]], axis=0)
        from_after = jnp.concatenate([g_extended[1:, :BLK], zero_grad], axis=0)
        g_tiles = g_tiles.at[:, :BLK].add(from_before)
        g_tiles = g_tiles.at[:, REG_DEV - BLK:].add(from_after)
        g_h = g_tiles.reshape(RCELLS, W).astype(jnp.bfloat16)
        g_forced, g_gain = norm_back(g_h)
        g_forced = (g_forced + cot_m.astype(jnp.float32)).astype(jnp.bfloat16)
        g_bound = jnp.dot(boundary.T, g_forced, preferred_element_type=jnp.float32)
        result = (forced + attended.reshape(RCELLS, W)).astype(jnp.bfloat16)
        parts = (lax.optimization_barrier(jnp.sum(gq, 0)), lax.optimization_barrier(jnp.sum(gk, 0)), lax.optimization_barrier(jnp.sum(gv, 0)), lax.optimization_barrier(jnp.sum(go, 0)), g_bound, g_gain)
        new_totals = tuple((old + part for old, part in zip(totals, parts)))
        return (new_totals, result)
    square = jnp.zeros((W, W), jnp.float32)
    start_totals = (square, square, square, square, square, jnp.zeros((W,), jnp.float32))
    totals, outputs = lax.scan(member, start_totals, (regional, cotangent))
    return (outputs, totals[0], totals[1], totals[2], totals[3], totals[4], totals[5])
```

```python
import functools
import math

import jax
import jax.numpy as jnp
from jax import lax
from jax.sharding import PartitionSpec as P

HEADS = 8
BLK = 128
NBR = 4


DOM = ("chip", "core")


def axis_count(axis):
    return lax.psum(1, axis)


def from_behind(block, axis, distance):
    devices = range(axis_count(axis))
    route = [((i - distance) % len(devices), i) for i in devices]
    return lax.ppermute(block, axis, route)


def padded(block, sides, width):
    for axis, dim in sides:
        count = axis_count(axis)
        forward = [(i, i + 1) for i in range(count - 1)]
        backward = [(target, source) for source, target in forward]
        low = lax.ppermute(
            lax.slice_in_dim(block, block.shape[dim] - width, None, axis=dim), axis, forward
        )
        high = lax.ppermute(lax.slice_in_dim(block, 0, width, axis=dim), axis, backward)
        block = jnp.concatenate([low, block, high], axis=dim)
    return block


def passed_along(value, axis, steps):
    count = axis_count(axis)
    leading, last = (max(0, -steps), min(count, count - steps))
    return lax.ppermute(value, axis, [(source, source + steps) for source in range(leading, last)])


def normalize(forced, norm_gain):
    inverse = lax.rsqrt(jnp.mean(forced * forced, axis=-1, keepdims=True) + 1e-06)
    return (forced * inverse * norm_gain).astype(jnp.bfloat16)


def attend_core(queries, key_rows, value_rows, neighbors):
    blocks = queries.shape[0] // BLK
    width = queries.shape[1]
    head_dim = width // HEADS
    query_blocks = queries.reshape(blocks, BLK, HEADS, head_dim)
    key_blocks = key_rows.reshape(blocks + 2, BLK, width)[neighbors].reshape(
        blocks, NBR * BLK, HEADS, head_dim
    )
    value_blocks = value_rows.reshape(blocks + 2, BLK, width)[neighbors].reshape(
        blocks, NBR * BLK, HEADS, head_dim
    )
    scores = jnp.einsum(
        "bqhd,bkhd->bhqk", query_blocks, key_blocks, preferred_element_type=jnp.float32
    ) * (1.0 / math.sqrt(head_dim))
    expo = jnp.exp(scores)
    probs = (expo / jnp.sum(expo, axis=-1, keepdims=True)).astype(jnp.bfloat16)
    mixed = jnp.einsum("bhqk,bkhd->bqhd", probs, value_blocks, preferred_element_type=jnp.float32)
    return mixed.reshape(blocks * BLK, width).astype(jnp.bfloat16)


def shards(
    global_latent,
    send_rows,
    regional,
    interp_index,
    interp_weight,
    neighbors,
    w_bound,
    w_query,
    w_key,
    w_value,
    w_output,
    norm_gain,
    cotangent,
):
    picked = global_latent[send_rows[0]]
    from_below = from_behind(picked[2], DOM, 1)
    from_above = from_behind(picked[0], DOM, -1)
    slot_table = jnp.concatenate([from_below, picked[1], from_above], axis=0)
    boundary = jnp.sum(
        interp_weight[:, :, None] * slot_table[interp_index].astype(jnp.float32), axis=1
    ).astype(jnp.bfloat16)
    forced = regional[0].astype(jnp.float32) + jnp.dot(
        boundary, w_bound, preferred_element_type=jnp.float32
    )
    hidden, norm_back = jax.vjp(normalize, forced, norm_gain)
    extended = padded(hidden, ((DOM, 0),), BLK)
    queries = jnp.dot(hidden, w_query, preferred_element_type=jnp.float32).astype(jnp.bfloat16)
    key_rows = jnp.dot(extended, w_key, preferred_element_type=jnp.float32).astype(jnp.bfloat16)
    value_rows = jnp.dot(extended, w_value, preferred_element_type=jnp.float32).astype(jnp.bfloat16)
    core = functools.partial(attend_core, neighbors=neighbors)
    mixed_heads, core_back = jax.vjp(core, queries, key_rows, value_rows)
    attended = jnp.dot(mixed_heads, w_output, preferred_element_type=jnp.float32)
    regional_out = (forced + attended).astype(jnp.bfloat16)[None]
    grads_out = cotangent[0]
    grad_output = jnp.dot(mixed_heads.T, grads_out, preferred_element_type=jnp.float32)
    g_mixed = jnp.dot(grads_out, w_output.T, preferred_element_type=jnp.float32).astype(
        jnp.bfloat16
    )
    g_queries, g_keys, g_values = core_back(g_mixed)
    grad_query = jnp.dot(hidden.T, g_queries, preferred_element_type=jnp.float32)
    grad_key = jnp.dot(extended.T, g_keys, preferred_element_type=jnp.float32)
    grad_value = jnp.dot(extended.T, g_values, preferred_element_type=jnp.float32)
    g_extended = jnp.dot(g_keys, w_key.T, preferred_element_type=jnp.float32) + jnp.dot(
        g_values, w_value.T, preferred_element_type=jnp.float32
    )
    tile_cells = hidden.shape[0]
    from_before = passed_along(
        g_extended[BLK + tile_cells :].astype(jnp.bfloat16), DOM, 1
    ).astype(jnp.float32)
    from_after = passed_along(g_extended[:BLK].astype(jnp.bfloat16), DOM, -1).astype(jnp.float32)
    g_hidden = (
        jnp.dot(g_queries, w_query.T, preferred_element_type=jnp.float32)
        + g_extended[BLK : BLK + tile_cells]
    )
    g_hidden = g_hidden.at[:BLK].add(from_before)
    g_hidden = g_hidden.at[tile_cells - BLK :].add(from_after)
    g_forced, grad_gain = norm_back(g_hidden.astype(jnp.bfloat16))
    g_forced = (g_forced + grads_out.astype(jnp.float32)).astype(jnp.bfloat16)
    grad_bound = jnp.dot(boundary.T, g_forced, preferred_element_type=jnp.float32)
    grad_query, grad_key, grad_value, grad_output, grad_bound, grad_gain = summed_everywhere(
        (grad_query, grad_key, grad_value, grad_output, grad_bound, grad_gain)
    )
    return (regional_out, grad_query, grad_key, grad_value, grad_output, grad_bound, grad_gain)


def swap_cores(value):
    return lax.ppermute(value, "core", [(0, 1), (1, 0)])


def halved(block, axis, distance):
    index = lax.axis_index(axis)
    count = axis_count(axis)
    half = block.shape[0] // 2
    bit = (index // distance) % 2
    keep = lax.dynamic_slice_in_dim(block, bit * half, half, 0)
    give = lax.dynamic_slice_in_dim(block, (1 - bit) * half, half, 0)
    return keep + lax.ppermute(give, axis, [(i, i ^ distance) for i in range(count)])


def doubled(block, axis, distance):
    index = lax.axis_index(axis)
    count = axis_count(axis)
    bit = (index // distance) % 2
    got = lax.ppermute(block, axis, [(i, i ^ distance) for i in range(count)])
    return jnp.concatenate(
        [jnp.where(bit == 0, block, got), jnp.where(bit == 0, got, block)], axis=0
    )


def bit_orders(chips, members):
    def bits(axis, count):
        return [(axis, 1 << k) for k in range(count.bit_length() - 1)]

    x_bits = bits("chip", 4)
    y_bits = [("chip", 4 * d) for _, d in bits("chip", chips // 4)]
    z_bits = bits("mem", members)
    groups = [x_bits, y_bits, z_bits]
    orders = []
    for shift in range(len(groups)):
        turn = groups[shift:] + groups[:shift]
        order = []
        for level in range(max(len(g) for g in groups)):
            order += [g[level] for g in turn if level < len(g)]
        orders.append(order)
    return orders


def core_halves(block):
    core = lax.axis_index("core")
    half = block.shape[0] // 2
    own = lax.dynamic_slice_in_dim(block, core * half, half, 0)
    other = lax.dynamic_slice_in_dim(block, (1 - core) * half, half, 0)
    return own, other


def summed_everywhere(parts):
    *squares, gain = parts
    width = gain.shape[-1]
    chips = axis_count("chip")
    members = axis_count("mem")
    orders = bit_orders(chips, members)
    depth = len(orders[0])
    gain_rows = 2 << depth
    gain_block = jnp.zeros((gain_rows, width), jnp.float32).at[0].set(gain)
    pieces = list(squares) + [gain_block]
    owns, others = zip(*[core_halves(piece) for piece in pieces])
    received = lax.ppermute(tuple(others), "core", [(0, 1), (1, 0)])
    sums = [own + got for own, got in zip(owns, received)]
    groups = [[0, 1], [2, 3], [4, 5]]
    slices = [jnp.concatenate([sums[j] for j in group], axis=0) for group in groups]
    for step in range(depth):
        slices = [halved(s, *order[step]) for s, order in zip(slices, orders)]
    slices = [s.astype(jnp.bfloat16) for s in slices]
    for step in reversed(range(depth)):
        slices = [doubled(s, *order[step]) for s, order in zip(slices, orders)]
    received = lax.ppermute(tuple(slices), "core", [(0, 1), (1, 0)])
    core = lax.axis_index("core")
    out = []
    for group, mine, theirs in zip(groups, slices, received):
        start = 0
        for j in group:
            size = owns[j].shape[0]
            a = mine[start : start + size]
            b = theirs[start : start + size]
            start += size
            whole = jnp.where(
                core == 0, jnp.concatenate([a, b], axis=0), jnp.concatenate([b, a], axis=0)
            )
            out.append(whole.astype(jnp.float32))
    out[-1] = out[-1][0]
    return tuple(out)


def solution(mesh):
    chips = mesh.shape["dom"] // 2
    devices = mesh.devices.reshape(chips, 2, mesh.shape["mem"])
    mesh = jax.sharding.Mesh(devices, ("chip", "core", "mem"))
    placed = (
        P(DOM, None),
        P(DOM, None, None),
        P("mem", DOM, None),
        P(DOM, None),
        P(DOM, None),
        P(DOM, None),
        P(),
        P(),
        P(),
        P(),
        P(),
        P(),
        P("mem", DOM, None),
    )
    return jax.shard_map(
        shards,
        mesh=mesh,
        in_specs=placed,
        out_specs=(P("mem", DOM, None), P(), P(), P(), P(), P(), P()),
        check_vma=False,
    )
```

```python
import functools
import math

import jax
import jax.numpy as jnp
from jax import lax
from jax.sharding import PartitionSpec as P

HEADS = 8
BLK = 128
NBR = 4


DOM = ("chip", "core")


def axis_count(axis):
    return lax.psum(1, axis)


def from_behind(block, axis, distance):
    devices = range(axis_count(axis))
    route = [((i - distance) % len(devices), i) for i in devices]
    return lax.ppermute(block, axis, route)


def padded(block, sides, width):
    for axis, dim in sides:
        count = axis_count(axis)
        forward = [(i, i + 1) for i in range(count - 1)]
        backward = [(target, source) for source, target in forward]
        low = lax.ppermute(
            lax.slice_in_dim(block, block.shape[dim] - width, None, axis=dim), axis, forward
        )
        high = lax.ppermute(lax.slice_in_dim(block, 0, width, axis=dim), axis, backward)
        block = jnp.concatenate([low, block, high], axis=dim)
    return block


def passed_along(value, axis, steps):
    count = axis_count(axis)
    leading, last = (max(0, -steps), min(count, count - steps))
    return lax.ppermute(value, axis, [(source, source + steps) for source in range(leading, last)])


def normalize(forced, norm_gain):
    inverse = lax.rsqrt(jnp.mean(forced * forced, axis=-1, keepdims=True) + 1e-06)
    return (forced * inverse * norm_gain).astype(jnp.bfloat16)


def attend_core(queries, key_rows, value_rows, neighbors):
    blocks = queries.shape[0] // BLK
    width = queries.shape[1]
    head_dim = width // HEADS
    query_blocks = queries.reshape(blocks, BLK, HEADS, head_dim)
    key_blocks = key_rows.reshape(blocks + 2, BLK, width)[neighbors].reshape(
        blocks, NBR * BLK, HEADS, head_dim
    )
    value_blocks = value_rows.reshape(blocks + 2, BLK, width)[neighbors].reshape(
        blocks, NBR * BLK, HEADS, head_dim
    )
    scores = jnp.einsum(
        "bqhd,bkhd->bhqk", query_blocks, key_blocks, preferred_element_type=jnp.float32
    ) * (1.0 / math.sqrt(head_dim))
    expo = jnp.exp(scores)
    probs = (expo / jnp.sum(expo, axis=-1, keepdims=True)).astype(jnp.bfloat16)
    mixed = jnp.einsum("bhqk,bkhd->bqhd", probs, value_blocks, preferred_element_type=jnp.float32)
    return mixed.reshape(blocks * BLK, width).astype(jnp.bfloat16)


def shards(
    global_latent,
    send_rows,
    regional,
    interp_index,
    interp_weight,
    neighbors,
    w_bound,
    w_query,
    w_key,
    w_value,
    w_output,
    norm_gain,
    cotangent,
):
    picked = global_latent[send_rows[0]]
    from_below = from_behind(picked[2], DOM, 1)
    from_above = from_behind(picked[0], DOM, -1)
    slot_table = jnp.concatenate([from_below, picked[1], from_above], axis=0)
    boundary = jnp.sum(
        interp_weight[:, :, None] * slot_table[interp_index].astype(jnp.float32), axis=1
    ).astype(jnp.bfloat16)
    forced = regional[0].astype(jnp.float32) + jnp.dot(
        boundary, w_bound, preferred_element_type=jnp.float32
    )
    hidden, norm_back = jax.vjp(normalize, forced, norm_gain)
    extended = padded(hidden, ((DOM, 0),), BLK)
    queries = jnp.dot(hidden, w_query, preferred_element_type=jnp.float32).astype(jnp.bfloat16)
    key_rows = jnp.dot(extended, w_key, preferred_element_type=jnp.float32).astype(jnp.bfloat16)
    value_rows = jnp.dot(extended, w_value, preferred_element_type=jnp.float32).astype(jnp.bfloat16)
    core = functools.partial(attend_core, neighbors=neighbors)
    mixed_heads, core_back = jax.vjp(core, queries, key_rows, value_rows)
    attended = jnp.dot(mixed_heads, w_output, preferred_element_type=jnp.float32)
    regional_out = (forced + attended).astype(jnp.bfloat16)[None]
    grads_out = cotangent[0]
    grad_output = jnp.dot(mixed_heads.T, grads_out, preferred_element_type=jnp.float32)
    g_mixed = jnp.dot(grads_out, w_output.T, preferred_element_type=jnp.float32).astype(
        jnp.bfloat16
    )
    g_queries, g_keys, g_values = core_back(g_mixed)
    grad_query = jnp.dot(hidden.T, g_queries, preferred_element_type=jnp.float32)
    grad_key = jnp.dot(extended.T, g_keys, preferred_element_type=jnp.float32)
    grad_value = jnp.dot(extended.T, g_values, preferred_element_type=jnp.float32)
    g_extended = jnp.dot(g_keys, w_key.T, preferred_element_type=jnp.float32) + jnp.dot(
        g_values, w_value.T, preferred_element_type=jnp.float32
    )
    tile_cells = hidden.shape[0]
    from_before = passed_along(
        g_extended[BLK + tile_cells :].astype(jnp.bfloat16), DOM, 1
    ).astype(jnp.float32)
    from_after = passed_along(g_extended[:BLK].astype(jnp.bfloat16), DOM, -1).astype(jnp.float32)
    g_hidden = (
        jnp.dot(g_queries, w_query.T, preferred_element_type=jnp.float32)
        + g_extended[BLK : BLK + tile_cells]
    )
    g_hidden = g_hidden.at[:BLK].add(from_before)
    g_hidden = g_hidden.at[tile_cells - BLK :].add(from_after)
    g_forced, grad_gain = norm_back(g_hidden.astype(jnp.bfloat16))
    g_forced = (g_forced + grads_out.astype(jnp.float32)).astype(jnp.bfloat16)
    grad_bound = jnp.dot(boundary.T, g_forced, preferred_element_type=jnp.float32)
    grad_query, grad_key, grad_value, grad_output, grad_bound, grad_gain = summed_everywhere(
        (grad_query, grad_key, grad_value, grad_output, grad_bound, grad_gain)
    )
    return (regional_out, grad_query, grad_key, grad_value, grad_output, grad_bound, grad_gain)


def swap_cores(value):
    return lax.ppermute(value, "core", [(0, 1), (1, 0)])


def halved(block, axis, distance):
    index = lax.axis_index(axis)
    count = axis_count(axis)
    half = block.shape[0] // 2
    bit = (index // distance) % 2
    keep = lax.dynamic_slice_in_dim(block, bit * half, half, 0)
    give = lax.dynamic_slice_in_dim(block, (1 - bit) * half, half, 0)
    return keep + lax.ppermute(give, axis, [(i, i ^ distance) for i in range(count)])


def doubled(block, axis, distance):
    index = lax.axis_index(axis)
    count = axis_count(axis)
    bit = (index // distance) % 2
    got = lax.ppermute(block, axis, [(i, i ^ distance) for i in range(count)])
    return jnp.concatenate(
        [jnp.where(bit == 0, block, got), jnp.where(bit == 0, got, block)], axis=0
    )


def bit_orders(chips, members):
    def bits(axis, count):
        return [(axis, 1 << k) for k in range(count.bit_length() - 1)]

    x_bits = bits("chip", 4)
    y_bits = [("chip", 4 * d) for _, d in bits("chip", chips // 4)]
    z_bits = bits("mem", members)
    groups = [x_bits, y_bits, z_bits]
    orders = []
    for shift in range(len(groups)):
        turn = groups[shift:] + groups[:shift]
        order = []
        for level in range(max(len(g) for g in groups)):
            order += [g[level] for g in turn if level < len(g)]
        orders.append(order)
    return orders


def core_halves(block):
    core = lax.axis_index("core")
    half = block.shape[0] // 2
    own = lax.dynamic_slice_in_dim(block, core * half, half, 0)
    other = lax.dynamic_slice_in_dim(block, (1 - core) * half, half, 0)
    return own, other


def summed_everywhere(parts):
    *squares, gain = parts
    width = gain.shape[-1]
    chips = axis_count("chip")
    members = axis_count("mem")
    orders = bit_orders(chips, members)
    depth = len(orders[0])
    gain_rows = 2 << depth
    gain_block = jnp.zeros((gain_rows, width), jnp.float32).at[0].set(gain)
    pieces = list(squares) + [gain_block]
    owns, others = zip(*[core_halves(piece) for piece in pieces])
    received = lax.ppermute(tuple(others), "core", [(0, 1), (1, 0)])
    sums = [own + got for own, got in zip(owns, received)]
    groups = [[0, 1], [2, 3], [4, 5]]
    slices = [jnp.concatenate([sums[j] for j in group], axis=0) for group in groups]
    lead = len(orders)
    for step in range(lead):
        slices = [halved(s, *order[step]) for s, order in zip(slices, orders)]
    sizes = [s.shape[0] for s in slices]
    block = jnp.concatenate(slices, axis=0)
    for bit in orders[0][lead:]:
        block = halved(block, *bit)
    block = block.astype(jnp.bfloat16)
    for bit in reversed(orders[0][lead:]):
        block = doubled(block, *bit)
    offsets = [sum(sizes[:k]) for k in range(len(sizes))]
    slices = [block[o : o + n] for o, n in zip(offsets, sizes)]
    for step in reversed(range(lead)):
        slices = [doubled(s, *order[step]) for s, order in zip(slices, orders)]
    received = lax.ppermute(tuple(slices), "core", [(0, 1), (1, 0)])
    core = lax.axis_index("core")
    out = []
    for group, mine, theirs in zip(groups, slices, received):
        start = 0
        for j in group:
            size = owns[j].shape[0]
            a = mine[start : start + size]
            b = theirs[start : start + size]
            start += size
            whole = jnp.where(
                core == 0, jnp.concatenate([a, b], axis=0), jnp.concatenate([b, a], axis=0)
            )
            out.append(whole.astype(jnp.float32))
    out[-1] = out[-1][0]
    return tuple(out)


def solution(mesh):
    chips = mesh.shape["dom"] // 2
    devices = mesh.devices.reshape(chips, 2, mesh.shape["mem"])
    mesh = jax.sharding.Mesh(devices, ("chip", "core", "mem"))
    placed = (
        P(DOM, None),
        P(DOM, None, None),
        P("mem", DOM, None),
        P(DOM, None),
        P(DOM, None),
        P(DOM, None),
        P(),
        P(),
        P(),
        P(),
        P(),
        P(),
        P("mem", DOM, None),
    )
    return jax.shard_map(
        shards,
        mesh=mesh,
        in_specs=placed,
        out_specs=(P("mem", DOM, None), P(), P(), P(), P(), P(), P()),
        check_vma=False,
    )
```

```python
import functools
import math

import jax
import jax.numpy as jnp
from jax import lax
from jax.sharding import PartitionSpec as P

HEADS = 8
BLK = 128
NBR = 4


DOM = ("chip", "core")


def axis_count(axis):
    return lax.psum(1, axis)


def from_behind(block, axis, distance):
    devices = range(axis_count(axis))
    route = [((i - distance) % len(devices), i) for i in devices]
    return lax.ppermute(block, axis, route)


def padded(block, sides, width):
    for axis, dim in sides:
        count = axis_count(axis)
        forward = [(i, i + 1) for i in range(count - 1)]
        backward = [(target, source) for source, target in forward]
        low = lax.ppermute(
            lax.slice_in_dim(block, block.shape[dim] - width, None, axis=dim), axis, forward
        )
        high = lax.ppermute(lax.slice_in_dim(block, 0, width, axis=dim), axis, backward)
        block = jnp.concatenate([low, block, high], axis=dim)
    return block


def passed_along(value, axis, steps):
    count = axis_count(axis)
    leading, last = (max(0, -steps), min(count, count - steps))
    return lax.ppermute(value, axis, [(source, source + steps) for source in range(leading, last)])


def normalize(forced, norm_gain):
    inverse = lax.rsqrt(jnp.mean(forced * forced, axis=-1, keepdims=True) + 1e-06)
    return (forced * inverse * norm_gain).astype(jnp.bfloat16)


def attend_core(queries, key_rows, value_rows, neighbors):
    blocks = queries.shape[0] // BLK
    width = queries.shape[1]
    head_dim = width // HEADS
    query_blocks = queries.reshape(blocks, BLK, HEADS, head_dim)
    key_blocks = key_rows.reshape(blocks + 2, BLK, width)[neighbors].reshape(
        blocks, NBR * BLK, HEADS, head_dim
    )
    value_blocks = value_rows.reshape(blocks + 2, BLK, width)[neighbors].reshape(
        blocks, NBR * BLK, HEADS, head_dim
    )
    scores = jnp.einsum(
        "bqhd,bkhd->bhqk", query_blocks, key_blocks, preferred_element_type=jnp.float32
    ) * (1.0 / math.sqrt(head_dim))
    expo = jnp.exp(scores)
    probs = (expo / jnp.sum(expo, axis=-1, keepdims=True)).astype(jnp.bfloat16)
    mixed = jnp.einsum("bhqk,bkhd->bqhd", probs, value_blocks, preferred_element_type=jnp.float32)
    return mixed.reshape(blocks * BLK, width).astype(jnp.bfloat16)


def shards(
    global_latent,
    send_rows,
    regional,
    interp_index,
    interp_weight,
    neighbors,
    w_bound,
    w_query,
    w_key,
    w_value,
    w_output,
    norm_gain,
    cotangent,
):
    picked = global_latent[send_rows[0]]
    from_below = from_behind(picked[2], DOM, 1)
    from_above = from_behind(picked[0], DOM, -1)
    slot_table = jnp.concatenate([from_below, picked[1], from_above], axis=0)
    boundary = jnp.sum(
        interp_weight[:, :, None] * slot_table[interp_index].astype(jnp.float32), axis=1
    ).astype(jnp.bfloat16)
    forced = regional[0].astype(jnp.float32) + jnp.dot(
        boundary, w_bound, preferred_element_type=jnp.float32
    )
    hidden, norm_back = jax.vjp(normalize, forced, norm_gain)
    extended = padded(hidden, ((DOM, 0),), BLK)
    queries = jnp.dot(hidden, w_query, preferred_element_type=jnp.float32).astype(jnp.bfloat16)
    key_rows = jnp.dot(extended, w_key, preferred_element_type=jnp.float32).astype(jnp.bfloat16)
    value_rows = jnp.dot(extended, w_value, preferred_element_type=jnp.float32).astype(jnp.bfloat16)
    core = functools.partial(attend_core, neighbors=neighbors)
    mixed_heads, core_back = jax.vjp(core, queries, key_rows, value_rows)
    attended = jnp.dot(mixed_heads, w_output, preferred_element_type=jnp.float32)
    regional_out = (forced + attended).astype(jnp.bfloat16)[None]
    grads_out = cotangent[0]
    grad_output = jnp.dot(mixed_heads.T, grads_out, preferred_element_type=jnp.float32)
    g_mixed = jnp.dot(grads_out, w_output.T, preferred_element_type=jnp.float32).astype(
        jnp.bfloat16
    )
    g_queries, g_keys, g_values = core_back(g_mixed)
    grad_query = jnp.dot(hidden.T, g_queries, preferred_element_type=jnp.float32)
    grad_key = jnp.dot(extended.T, g_keys, preferred_element_type=jnp.float32)
    grad_value = jnp.dot(extended.T, g_values, preferred_element_type=jnp.float32)
    g_extended = jnp.dot(g_keys, w_key.T, preferred_element_type=jnp.float32) + jnp.dot(
        g_values, w_value.T, preferred_element_type=jnp.float32
    )
    tile_cells = hidden.shape[0]
    from_before = passed_along(
        g_extended[BLK + tile_cells :].astype(jnp.bfloat16), DOM, 1
    ).astype(jnp.float32)
    from_after = passed_along(g_extended[:BLK].astype(jnp.bfloat16), DOM, -1).astype(jnp.float32)
    g_hidden = (
        jnp.dot(g_queries, w_query.T, preferred_element_type=jnp.float32)
        + g_extended[BLK : BLK + tile_cells]
    )
    g_hidden = g_hidden.at[:BLK].add(from_before)
    g_hidden = g_hidden.at[tile_cells - BLK :].add(from_after)
    g_forced, grad_gain = norm_back(g_hidden.astype(jnp.bfloat16))
    g_forced = (g_forced + grads_out.astype(jnp.float32)).astype(jnp.bfloat16)
    grad_bound = jnp.dot(boundary.T, g_forced, preferred_element_type=jnp.float32)
    grad_query, grad_key, grad_value, grad_output, grad_bound, grad_gain = summed_everywhere(
        (grad_query, grad_key, grad_value, grad_output, grad_bound, grad_gain)
    )
    return (regional_out, grad_query, grad_key, grad_value, grad_output, grad_bound, grad_gain)


def swap_cores(value):
    return lax.ppermute(value, "core", [(0, 1), (1, 0)])


def halved(block, axis, distance):
    index = lax.axis_index(axis)
    count = axis_count(axis)
    half = block.shape[0] // 2
    bit = (index // distance) % 2
    keep = lax.dynamic_slice_in_dim(block, bit * half, half, 0)
    give = lax.dynamic_slice_in_dim(block, (1 - bit) * half, half, 0)
    return keep + lax.ppermute(give, axis, [(i, i ^ distance) for i in range(count)])


def doubled(block, axis, distance):
    index = lax.axis_index(axis)
    count = axis_count(axis)
    bit = (index // distance) % 2
    got = lax.ppermute(block, axis, [(i, i ^ distance) for i in range(count)])
    return jnp.concatenate(
        [jnp.where(bit == 0, block, got), jnp.where(bit == 0, got, block)], axis=0
    )


def bit_orders(chips, members):
    def bits(axis, count):
        return [(axis, 1 << k) for k in range(count.bit_length() - 1)]

    x_bits = bits("chip", 4)
    y_bits = [("chip", 4 * d) for _, d in bits("chip", chips // 4)]
    z_bits = bits("mem", members)
    groups = [x_bits, y_bits, z_bits]
    orders = []
    for shift in range(len(groups)):
        turn = groups[shift:] + groups[:shift]
        order = []
        for level in range(max(len(g) for g in groups)):
            order += [g[level] for g in turn if level < len(g)]
        orders.append(order)
    return orders


def core_halves(block):
    core = lax.axis_index("core")
    half = block.shape[0] // 2
    own = lax.dynamic_slice_in_dim(block, core * half, half, 0)
    other = lax.dynamic_slice_in_dim(block, (1 - core) * half, half, 0)
    return own, other


def summed_everywhere(parts):
    *squares, gain = parts
    width = gain.shape[-1]
    chips = axis_count("chip")
    members = axis_count("mem")
    orders = bit_orders(chips, members)
    depth = len(orders[0])
    gain_rows = 2 << depth
    gain_block = jnp.zeros((gain_rows, width), jnp.float32).at[0].set(gain)
    pieces = list(squares) + [gain_block]
    owns, others = zip(*[core_halves(piece) for piece in pieces])
    received = lax.ppermute(tuple(others), "core", [(0, 1), (1, 0)])
    sums = [own + got for own, got in zip(owns, received)]
    groups = [[0, 1], [2, 3], [4, 5]]
    slices = [jnp.concatenate([sums[j] for j in group], axis=0) for group in groups]
    lead = len(orders)
    for step in range(lead):
        slices = [halved(s, *order[step]) for s, order in zip(slices, orders)]
    sizes = [s.shape[0] for s in slices]
    block = jnp.concatenate(slices, axis=0)
    tail = [bit for bit in orders[0][lead:] if bit[0] == "chip"]
    for bit in tail:
        block = halved(block, *bit)
    for axis, distance in orders[0][lead:]:
        if axis != "chip":
            route = [(i, i ^ distance) for i in range(axis_count(axis))]
            block = block + lax.ppermute(block, axis, route)
    block = block.astype(jnp.bfloat16)
    for bit in reversed(tail):
        block = doubled(block, *bit)
    offsets = [sum(sizes[:k]) for k in range(len(sizes))]
    slices = [block[o : o + n] for o, n in zip(offsets, sizes)]
    for step in reversed(range(lead)):
        slices = [doubled(s, *order[step]) for s, order in zip(slices, orders)]
    received = lax.ppermute(tuple(slices), "core", [(0, 1), (1, 0)])
    core = lax.axis_index("core")
    out = []
    for group, mine, theirs in zip(groups, slices, received):
        start = 0
        for j in group:
            size = owns[j].shape[0]
            a = mine[start : start + size]
            b = theirs[start : start + size]
            start += size
            whole = jnp.where(
                core == 0, jnp.concatenate([a, b], axis=0), jnp.concatenate([b, a], axis=0)
            )
            out.append(whole.astype(jnp.float32))
    out[-1] = out[-1][0]
    return tuple(out)


def solution(mesh):
    chips = mesh.shape["dom"] // 2
    devices = mesh.devices.reshape(chips, 2, mesh.shape["mem"])
    mesh = jax.sharding.Mesh(devices, ("chip", "core", "mem"))
    placed = (
        P(DOM, None),
        P(DOM, None, None),
        P("mem", DOM, None),
        P(DOM, None),
        P(DOM, None),
        P(DOM, None),
        P(),
        P(),
        P(),
        P(),
        P(),
        P(),
        P("mem", DOM, None),
    )
    return jax.shard_map(
        shards,
        mesh=mesh,
        in_specs=placed,
        out_specs=(P("mem", DOM, None), P(), P(), P(), P(), P(), P()),
        check_vma=False,
    )
```

```python
import functools
import math

import jax
import jax.numpy as jnp
from jax import lax
from jax.sharding import PartitionSpec as P

HEADS = 8
BLK = 128
NBR = 4


DOM = ("chip", "core")


def axis_count(axis):
    return lax.psum(1, axis)


def from_behind(block, axis, distance):
    devices = range(axis_count(axis))
    route = [((i - distance) % len(devices), i) for i in devices]
    return lax.ppermute(block, axis, route)


def padded(block, sides, width):
    for axis, dim in sides:
        count = axis_count(axis)
        forward = [(i, i + 1) for i in range(count - 1)]
        backward = [(target, source) for source, target in forward]
        low = lax.ppermute(
            lax.slice_in_dim(block, block.shape[dim] - width, None, axis=dim), axis, forward
        )
        high = lax.ppermute(lax.slice_in_dim(block, 0, width, axis=dim), axis, backward)
        block = jnp.concatenate([low, block, high], axis=dim)
    return block


def passed_along(value, axis, steps):
    count = axis_count(axis)
    leading, last = (max(0, -steps), min(count, count - steps))
    return lax.ppermute(value, axis, [(source, source + steps) for source in range(leading, last)])


def normalize(forced, norm_gain):
    inverse = lax.rsqrt(jnp.mean(forced * forced, axis=-1, keepdims=True) + 1e-06)
    return (forced * inverse * norm_gain).astype(jnp.bfloat16)


def attend_core(queries, key_rows, value_rows, neighbors):
    blocks = queries.shape[0] // BLK
    width = queries.shape[1]
    head_dim = width // HEADS
    query_blocks = queries.reshape(blocks, BLK, HEADS, head_dim)
    key_blocks = key_rows.reshape(blocks + 2, BLK, width)[neighbors].reshape(
        blocks, NBR * BLK, HEADS, head_dim
    )
    value_blocks = value_rows.reshape(blocks + 2, BLK, width)[neighbors].reshape(
        blocks, NBR * BLK, HEADS, head_dim
    )
    scores = jnp.einsum(
        "bqhd,bkhd->bhqk", query_blocks, key_blocks, preferred_element_type=jnp.float32
    ) * (1.0 / math.sqrt(head_dim))
    expo = jnp.exp(scores)
    probs = (expo / jnp.sum(expo, axis=-1, keepdims=True)).astype(jnp.bfloat16)
    mixed = jnp.einsum("bhqk,bkhd->bqhd", probs, value_blocks, preferred_element_type=jnp.float32)
    return mixed.reshape(blocks * BLK, width).astype(jnp.bfloat16)


def shards(
    global_latent,
    send_rows,
    regional,
    interp_index,
    interp_weight,
    neighbors,
    w_bound,
    w_query,
    w_key,
    w_value,
    w_output,
    norm_gain,
    cotangent,
):
    picked = global_latent[send_rows[0]]
    from_below = from_behind(picked[2], DOM, 1)
    from_above = from_behind(picked[0], DOM, -1)
    slot_table = jnp.concatenate([from_below, picked[1], from_above], axis=0)
    boundary = jnp.sum(
        interp_weight[:, :, None] * slot_table[interp_index].astype(jnp.float32), axis=1
    ).astype(jnp.bfloat16)
    forced = regional[0].astype(jnp.float32) + jnp.dot(
        boundary, w_bound, preferred_element_type=jnp.float32
    )
    hidden, norm_back = jax.vjp(normalize, forced, norm_gain)
    extended = padded(hidden, ((DOM, 0),), BLK)
    queries = jnp.dot(hidden, w_query, preferred_element_type=jnp.float32).astype(jnp.bfloat16)
    key_rows = jnp.dot(extended, w_key, preferred_element_type=jnp.float32).astype(jnp.bfloat16)
    value_rows = jnp.dot(extended, w_value, preferred_element_type=jnp.float32).astype(jnp.bfloat16)
    core = functools.partial(attend_core, neighbors=neighbors)
    mixed_heads, core_back = jax.vjp(core, queries, key_rows, value_rows)
    attended = jnp.dot(mixed_heads, w_output, preferred_element_type=jnp.float32)
    regional_out = (forced + attended).astype(jnp.bfloat16)[None]
    grads_out = cotangent[0]
    grad_output = jnp.dot(mixed_heads.T, grads_out, preferred_element_type=jnp.float32)
    g_mixed = jnp.dot(grads_out, w_output.T, preferred_element_type=jnp.float32).astype(
        jnp.bfloat16
    )
    g_queries, g_keys, g_values = core_back(g_mixed)
    grad_query = jnp.dot(hidden.T, g_queries, preferred_element_type=jnp.float32)
    grad_key = jnp.dot(extended.T, g_keys, preferred_element_type=jnp.float32)
    grad_value = jnp.dot(extended.T, g_values, preferred_element_type=jnp.float32)
    g_extended = jnp.dot(g_keys, w_key.T, preferred_element_type=jnp.float32) + jnp.dot(
        g_values, w_value.T, preferred_element_type=jnp.float32
    )
    tile_cells = hidden.shape[0]
    from_before = passed_along(
        g_extended[BLK + tile_cells :].astype(jnp.bfloat16), DOM, 1
    ).astype(jnp.float32)
    from_after = passed_along(g_extended[:BLK].astype(jnp.bfloat16), DOM, -1).astype(jnp.float32)
    g_hidden = (
        jnp.dot(g_queries, w_query.T, preferred_element_type=jnp.float32)
        + g_extended[BLK : BLK + tile_cells]
    )
    g_hidden = g_hidden.at[:BLK].add(from_before)
    g_hidden = g_hidden.at[tile_cells - BLK :].add(from_after)
    g_forced, grad_gain = norm_back(g_hidden.astype(jnp.bfloat16))
    g_forced = (g_forced + grads_out.astype(jnp.float32)).astype(jnp.bfloat16)
    grad_bound = jnp.dot(boundary.T, g_forced, preferred_element_type=jnp.float32)
    grad_query, grad_key, grad_value, grad_output, grad_bound, grad_gain = summed_everywhere(
        (grad_query, grad_key, grad_value, grad_output, grad_bound, grad_gain)
    )
    return (regional_out, grad_query, grad_key, grad_value, grad_output, grad_bound, grad_gain)


def swap_cores(value):
    return lax.ppermute(value, "core", [(0, 1), (1, 0)])


def halved(block, axis, distance):
    index = lax.axis_index(axis)
    count = axis_count(axis)
    half = block.shape[0] // 2
    bit = (index // distance) % 2
    keep = lax.dynamic_slice_in_dim(block, bit * half, half, 0)
    give = lax.dynamic_slice_in_dim(block, (1 - bit) * half, half, 0)
    return keep + lax.ppermute(give, axis, [(i, i ^ distance) for i in range(count)])


def doubled(block, axis, distance):
    index = lax.axis_index(axis)
    count = axis_count(axis)
    bit = (index // distance) % 2
    got = lax.ppermute(block, axis, [(i, i ^ distance) for i in range(count)])
    return jnp.concatenate(
        [jnp.where(bit == 0, block, got), jnp.where(bit == 0, got, block)], axis=0
    )


def bit_orders(chips, members):
    def bits(axis, count):
        return [(axis, 1 << k) for k in range(count.bit_length() - 1)]

    x_bits = bits("chip", 4)
    y_bits = [("chip", 4 * d) for _, d in bits("chip", chips // 4)]
    z_bits = bits("mem", members)
    groups = [x_bits, y_bits, z_bits]
    orders = []
    for shift in range(len(groups)):
        turn = groups[shift:] + groups[:shift]
        order = []
        for level in range(max(len(g) for g in groups)):
            order += [g[level] for g in turn if level < len(g)]
        orders.append(order)
    return orders


def core_halves(block):
    core = lax.axis_index("core")
    half = block.shape[0] // 2
    own = lax.dynamic_slice_in_dim(block, core * half, half, 0)
    other = lax.dynamic_slice_in_dim(block, (1 - core) * half, half, 0)
    return own, other


def summed_everywhere(parts):
    *squares, gain = parts
    width = gain.shape[-1]
    chips = axis_count("chip")
    members = axis_count("mem")
    orders = bit_orders(chips, members)
    depth = len(orders[0])
    gain_rows = 2 << depth
    gain_block = jnp.zeros((gain_rows, width), jnp.float32).at[0].set(gain)
    pieces = list(squares) + [gain_block]
    owns, others = zip(*[core_halves(piece) for piece in pieces])
    received = lax.ppermute(tuple(others), "core", [(0, 1), (1, 0)])
    sums = [own + got for own, got in zip(owns, received)]
    groups = [[0, 1], [2, 3], [4, 5]]
    slices = [jnp.concatenate([sums[j] for j in group], axis=0) for group in groups]
    lead = len(orders)
    for step in range(lead):
        slices = [halved(s, *order[step]) for s, order in zip(slices, orders)]
    sizes = [s.shape[0] for s in slices]
    block = jnp.concatenate(slices, axis=0)
    tail = [bit for bit in orders[0][lead:] if bit[0] == "chip"][:1]
    for bit in tail:
        block = halved(block, *bit)
    for axis, distance in orders[0][lead:]:
        if (axis, distance) not in tail:
            route = [(i, i ^ distance) for i in range(axis_count(axis))]
            block = block + lax.ppermute(block, axis, route)
    block = block.astype(jnp.bfloat16)
    for bit in reversed(tail):
        block = doubled(block, *bit)
    offsets = [sum(sizes[:k]) for k in range(len(sizes))]
    slices = [block[o : o + n] for o, n in zip(offsets, sizes)]
    for step in reversed(range(lead)):
        slices = [doubled(s, *order[step]) for s, order in zip(slices, orders)]
    received = lax.ppermute(tuple(slices), "core", [(0, 1), (1, 0)])
    core = lax.axis_index("core")
    out = []
    for group, mine, theirs in zip(groups, slices, received):
        start = 0
        for j in group:
            size = owns[j].shape[0]
            a = mine[start : start + size]
            b = theirs[start : start + size]
            start += size
            whole = jnp.where(
                core == 0, jnp.concatenate([a, b], axis=0), jnp.concatenate([b, a], axis=0)
            )
            out.append(whole.astype(jnp.float32))
    out[-1] = out[-1][0]
    return tuple(out)


def solution(mesh):
    chips = mesh.shape["dom"] // 2
    devices = mesh.devices.reshape(chips, 2, mesh.shape["mem"])
    mesh = jax.sharding.Mesh(devices, ("chip", "core", "mem"))
    placed = (
        P(DOM, None),
        P(DOM, None, None),
        P("mem", DOM, None),
        P(DOM, None),
        P(DOM, None),
        P(DOM, None),
        P(),
        P(),
        P(),
        P(),
        P(),
        P(),
        P("mem", DOM, None),
    )
    return jax.shard_map(
        shards,
        mesh=mesh,
        in_specs=placed,
        out_specs=(P("mem", DOM, None), P(), P(), P(), P(), P(), P()),
        check_vma=False,
    )
```
